128 devices in a mesh: row: 8 (over x, core), col: 4 (over z), depth: 4 (over y).
Axes of the slice: x: 4, y: 4, z: 4, core: 2. Of those that a mesh axis runs over, the one named last changes fastest.
Arguments:
- tokens: bfloat16 [1024, 8192], P(('col', 'depth'), 'row'), may hold values from -6 to 6
- gate_weight: bfloat16 [8192, 14336], P('row', ('col', 'depth')), may hold values from -0.109375 to 0.109375
- up_weight: bfloat16 [8192, 14336], P('row', ('col', 'depth')), may hold values from -0.109375 to 0.109375
- down_weight: bfloat16 [14336, 8192], P(('col', 'depth'), 'row'), may hold values from -0.078125 to 0.078125
- gate_mask: int32 [64, 112], P('row', ('col', 'depth')), may hold values 0 or 1
- up_mask: int32 [64, 112], P('row', ('col', 'depth')), may hold values 0 or 1
- down_mask: int32 [112, 64], P(('col', 'depth'), 'row'), may hold values 0 or 1
- grad_out: bfloat16 [1024, 8192], P(('col', 'depth'), 'row'), may hold values from -1.5 to 1.5
Outputs:
- mixed: bfloat16 [1024, 8192], P(('col', 'depth'), 'row')
- grad_tokens: bfloat16 [1024, 8192], P(('col', 'depth'), 'row')
- grad_gate_weight: bfloat16 [8192, 14336], P('row', ('col', 'depth'))
- grad_up_weight: bfloat16 [8192, 14336], P('row', ('col', 'depth'))
- grad_down_weight: bfloat16 [14336, 8192], P(('col', 'depth'), 'row')
The draws below stay inside these ranges and needn't reach their ends.
Inputs may be any that keep to these rules, and one draw needn't show every extreme that they name: `gate_mask`: 1 keeps the 128 x 128 block of the gate projection, 0 zeroes it. `up_mask`: 1 keeps the 128 x 128 block of the up projection, 0 zeroes it. `down_mask`: 1 keeps the 128 x 128 block of the down projection, 0 zeroes it.
All inputs are finite; a program needn't handle non-finite values.
Results may differ from the reference program's by a relative error of at most 0.015.
Values may be sent and summed in bfloat16 or wider, within the bound.
No kernel may reach another device: no remote copies, remote signals or barrier semaphores. Data moves between devices by JAX's collectives and lax.ppermute only.
A program may use at most 128 MiB of HBM per device.

```python
import jax
import jax.numpy as jnp
from jax import lax

D = 8192
FF = 14336
BLK = 128
TOKENS = 1024


def plant(result, rng, least, high):
    longest = result.shape.index(max(result.shape))
    spots = []
    for shift in (0, 1):
        where = [jax.random.randint(jax.random.fold_in(rng, axis), (), 0, length) for axis, length in enumerate(result.shape)]
        where[longest] = (where[longest] + shift) % result.shape[longest]
        spots.append(tuple(where))
    return result.at[spots[0]].set(least).at[spots[1]].set(high)


def block_levels(key, shape, pieces, low, largest):
    def one(position, parts):
        draws = jax.random.uniform(jax.random.fold_in(jax.random.fold_in(key, 6), position), (parts,), jnp.float32, low / len(pieces), largest / len(pieces))
        return jnp.repeat(jnp.exp(draws), shape[position] // parts).reshape((-1,) + (1,) * (len(shape) - position - 1))

    level = one(*pieces[0])
    for cut in pieces[1:]:
        level = level * one(*cut)
    return level


def bell_draw(stream_key, dims, deviation, bound, cuts=(), held_as=jnp.bfloat16):
    array = jax.random.normal(stream_key, dims, jnp.float32) * deviation
    if len(cuts) > 0:
        array = block_levels(stream_key, dims, cuts, -0.22, 0.18) * array
    return jnp.clip(array, min=-bound, max=bound).astype(held_as)


def setup_inputs(seed: int = 0) -> dict:
    keys = jax.random.split(jax.random.key(seed), 9)
    tokens = bell_draw(keys[0], (TOKENS, D), 1.0, 6.0, ((0, 16), (1, 8)))
    gate_weight = bell_draw(keys[1], (D, FF), (2 * D // 5) ** -0.5, 0.109375, ((0, 8), (1, 16)))
    up_weight = bell_draw(keys[2], (D, FF), (2 * D // 5) ** -0.5, 0.109375, ((0, 8), (1, 16)))
    down_weight = bell_draw(keys[3], (FF, D), (2 * FF // 5) ** -0.5, 0.078125, ((0, 16), (1, 8)))
    gate_mask = plant((jax.random.randint(keys[4], (D // BLK, FF // BLK), 0, 5) < 2).astype(jnp.int32), jax.random.fold_in(keys[4], 1), 0, 1)
    up_mask = plant((jax.random.randint(keys[5], (D // BLK, FF // BLK), 0, 5) < 2).astype(jnp.int32), jax.random.fold_in(keys[5], 1), 0, 1)
    down_mask = plant((jax.random.randint(keys[6], (FF // BLK, D // BLK), 0, 5) < 2).astype(jnp.int32), jax.random.fold_in(keys[6], 1), 0, 1)
    grad_out = bell_draw(keys[7], (TOKENS, D), 0.25, 1.5, ((0, 16), (1, 8)))
    return dict(tokens=tokens, gate_weight=gate_weight, up_weight=up_weight, down_weight=down_weight, gate_mask=gate_mask, up_mask=up_mask, down_mask=down_mask, grad_out=grad_out)


def expand(mask):
    return jnp.repeat(jnp.repeat(mask, BLK, axis=0), BLK, axis=1) > 0


def reference(tokens, gate_weight, up_weight, down_weight, gate_mask, up_mask, down_mask, grad_out):
    keep_gate = expand(gate_mask)
    keep_up = expand(up_mask)
    keep_down = expand(down_mask)
    kept_gate = jnp.where(keep_gate, gate_weight, jnp.zeros_like(gate_weight))
    kept_up = jnp.where(keep_up, up_weight, jnp.zeros_like(up_weight))
    kept_down = jnp.where(keep_down, down_weight, jnp.zeros_like(down_weight))
    gate = jnp.dot(tokens, kept_gate, preferred_element_type=jnp.float32)
    up = jnp.dot(tokens, kept_up, preferred_element_type=jnp.float32)
    sig = jax.nn.sigmoid(gate)
    act = (gate * sig * up).astype(jnp.bfloat16)
    mixed = jnp.dot(act, kept_down, preferred_element_type=jnp.float32).astype(jnp.bfloat16)
    inner = (((0,), (0,)), ((), ()))
    outer = (((1,), (1,)), ((), ()))
    grad_down = lax.dot_general(act, grad_out, inner, preferred_element_type=jnp.float32)
    grad_down_weight = jnp.where(keep_down, grad_down, jnp.float32(0.0)).astype(jnp.bfloat16)
    grad_act = lax.dot_general(grad_out, kept_down, outer, preferred_element_type=jnp.float32)
    grad_gate = (grad_act * up * sig * (1.0 + gate * (1.0 - sig))).astype(jnp.bfloat16)
    grad_up = (grad_act * gate * sig).astype(jnp.bfloat16)
    grad_g = lax.dot_general(tokens, grad_gate, inner, preferred_element_type=jnp.float32)
    grad_u = lax.dot_general(tokens, grad_up, inner, preferred_element_type=jnp.float32)
    grad_gate_weight = jnp.where(keep_gate, grad_g, jnp.float32(0.0)).astype(jnp.bfloat16)
    grad_up_weight = jnp.where(keep_up, grad_u, jnp.float32(0.0)).astype(jnp.bfloat16)
    grad_in = lax.dot_general(grad_gate, kept_gate, outer, preferred_element_type=jnp.float32)
    grad_in = grad_in + lax.dot_general(grad_up, kept_up, outer, preferred_element_type=jnp.float32)
    grad_tokens = grad_in.astype(jnp.bfloat16)
    return (mixed, grad_tokens, grad_gate_weight, grad_up_weight, grad_down_weight)
```

```python
import jax
import jax.numpy as jnp
from jax import lax
from jax.sharding import PartitionSpec as P

BLK = 128


def expand(mask):
    return jnp.repeat(jnp.repeat(mask, BLK, axis=0), BLK, axis=1) > 0


def swiglu(sums):
    width = sums.shape[1] // 2
    gate = sums[:, :width]
    up = sums[:, width:]
    sig = jax.nn.sigmoid(gate)
    return (gate * sig * up).astype(jnp.bfloat16)


def swiglu_back(sums, grad_act):
    width = sums.shape[1] // 2
    gate = sums[:, :width]
    up = sums[:, width:]
    sig = jax.nn.sigmoid(gate)
    grad_gate = grad_act * up * sig * (1.0 + gate * (1.0 - sig))
    grad_up = grad_act * gate * sig
    return jnp.concatenate([grad_gate, grad_up], axis=1).astype(jnp.bfloat16)


def row_sums(term, rows):
    return lax.psum_scatter(
        term(jnp.int32(0), lax.axis_size("row") * rows), "row", scatter_dimension=0, tiled=True
    )


def row_gather(block):
    return lax.all_gather(block, "row", axis=0, tiled=True)


def group_sums(term, rows):
    parts = lax.axis_size(("col", "depth"))
    full = term(jnp.int32(0), rows * parts).astype(jnp.bfloat16)
    pieces = lax.all_to_all(full.reshape((parts, rows) + full.shape[1:]), ("col", "depth"), 0, 0)
    return jnp.sum(pieces.astype(jnp.float32), axis=0)


def group_gather(block):
    parts = lax.axis_size(("col", "depth"))
    copies = jnp.broadcast_to(block[None], (parts,) + block.shape)
    pieces = lax.all_to_all(copies, ("col", "depth"), 0, 0)
    return pieces.reshape((parts * block.shape[0],) + block.shape[1:])


def local(tokens, gate_weight, up_weight, down_weight, gate_mask, up_mask, down_mask, grad_out):
    zero_value = jnp.zeros((), jnp.bfloat16)
    keep_gate = expand(gate_mask)
    keep_up = expand(up_mask)
    keep_down = expand(down_mask)
    w_both = jnp.concatenate(
        [jnp.where(keep_gate, gate_weight, zero_value), jnp.where(keep_up, up_weight, zero_value)],
        axis=1,
    )
    w_down = jnp.where(keep_down, down_weight, zero_value)
    both_all = group_gather(jnp.concatenate([tokens, grad_out], axis=1))
    x_all = both_all[:, : tokens.shape[1]]
    grad_all = both_all[:, tokens.shape[1] :]
    total = x_all.shape[0]
    split_rows = total // lax.axis_size("row")
    own_rows = tokens.shape[0]
    inner = (((0,), (0,)), ((), ()))
    outer = (((1,), (1,)), ((), ()))

    def hidden_term(start, count):
        return jnp.dot(x_all, w_both, preferred_element_type=jnp.float32)

    def act_term(start, count):
        return lax.dot_general(grad_all, w_down, outer, preferred_element_type=jnp.float32)

    sums = row_sums(hidden_term, split_rows)
    act_all = row_gather(swiglu(sums))

    def out_term(start, count):
        return jnp.dot(act_all, w_down, preferred_element_type=jnp.float32)

    mixed = group_sums(out_term, own_rows).astype(jnp.bfloat16)
    grad_down = lax.dot_general(act_all, grad_all, inner, preferred_element_type=jnp.float32)
    grad_down_weight = jnp.where(keep_down, grad_down, jnp.float32(0.0)).astype(jnp.bfloat16)
    grad_act = row_sums(act_term, split_rows)
    grads_all = row_gather(swiglu_back(sums, grad_act))
    grad_both = lax.dot_general(x_all, grads_all, inner, preferred_element_type=jnp.float32)
    width = grad_both.shape[1] // 2
    grad_gate_weight = jnp.where(keep_gate, grad_both[:, :width], jnp.float32(0.0)).astype(
        jnp.bfloat16
    )
    grad_up_weight = jnp.where(keep_up, grad_both[:, width:], jnp.float32(0.0)).astype(jnp.bfloat16)

    def input_term(start, count):
        return lax.dot_general(grads_all, w_both, outer, preferred_element_type=jnp.float32)

    grad_tokens = group_sums(input_term, own_rows).astype(jnp.bfloat16)
    return (mixed, grad_tokens, grad_gate_weight, grad_up_weight, grad_down_weight)


def solution(mesh):
    return jax.shard_map(
        local,
        mesh=mesh,
        in_specs=(
            P(("col", "depth"), "row"),
            P("row", ("col", "depth")),
            P("row", ("col", "depth")),
            P(("col", "depth"), "row"),
            P("row", ("col", "depth")),
            P("row", ("col", "depth")),
            P(("col", "depth"), "row"),
            P(("col", "depth"), "row"),
        ),
        out_specs=(
            P(("col", "depth"), "row"),
            P(("col", "depth"), "row"),
            P("row", ("col", "depth")),
            P("row", ("col", "depth")),
            P(("col", "depth"), "row"),
        ),
        check_vma=False,
    )
```

```python
import jax
import jax.numpy as jnp
from jax import lax
from jax.sharding import PartitionSpec as P

BLK = 128


def expand(mask):
    return jnp.repeat(jnp.repeat(mask, BLK, axis=0), BLK, axis=1) > 0


def swiglu(sums):
    width = sums.shape[1] // 2
    gate = sums[:, :width]
    up = sums[:, width:]
    sig = jax.nn.sigmoid(gate)
    return (gate * sig * up).astype(jnp.bfloat16)


def swiglu_back(sums, grad_act):
    width = sums.shape[1] // 2
    gate = sums[:, :width]
    up = sums[:, width:]
    sig = jax.nn.sigmoid(gate)
    grad_gate = grad_act * up * sig * (1.0 + gate * (1.0 - sig))
    grad_up = grad_act * gate * sig
    return jnp.concatenate([grad_gate, grad_up], axis=1).astype(jnp.bfloat16)


def row_sums(term, rows):
    return lax.psum_scatter(
        term(jnp.int32(0), lax.axis_size("row") * rows), "row", scatter_dimension=0, tiled=True
    )


def row_gather(block):
    return lax.all_gather(block, "row", axis=0, tiled=True)


def group_sums(term, rows):
    parts = lax.axis_size(("col", "depth"))
    full = term(jnp.int32(0), rows * parts).astype(jnp.bfloat16)
    pieces = lax.all_to_all(full.reshape((parts, rows) + full.shape[1:]), ("col", "depth"), 0, 0)
    return jnp.sum(pieces.astype(jnp.float32), axis=0)


def group_gather(block):
    parts = lax.axis_size(("col", "depth"))
    copies = jnp.broadcast_to(block[None], (parts,) + block.shape)
    pieces = lax.all_to_all(copies, ("col", "depth"), 0, 0)
    return pieces.reshape((parts * block.shape[0],) + block.shape[1:])


def local(tokens, gate_weight, up_weight, down_weight, gate_mask, up_mask, down_mask, grad_out):
    zero_value = jnp.zeros((), jnp.bfloat16)
    keep_gate = expand(gate_mask)
    keep_up = expand(up_mask)
    keep_down = expand(down_mask)
    w_both = jnp.concatenate(
        [jnp.where(keep_gate, gate_weight, zero_value), jnp.where(keep_up, up_weight, zero_value)],
        axis=1,
    )
    w_down = jnp.where(keep_down, down_weight, zero_value)
    grad_all = group_gather(grad_out)
    x_all = group_gather(tokens)
    total = x_all.shape[0]
    split_rows = total // lax.axis_size("row")
    own_rows = tokens.shape[0]
    inner = (((0,), (0,)), ((), ()))
    outer = (((1,), (1,)), ((), ()))

    def hidden_term(start, count):
        return jnp.dot(x_all, w_both, preferred_element_type=jnp.float32)

    def act_term(start, count):
        return lax.dot_general(grad_all, w_down, outer, preferred_element_type=jnp.float32)

    sums = row_sums(hidden_term, split_rows)
    act_all = row_gather(swiglu(sums))

    def out_term(start, count):
        return jnp.dot(act_all, w_down, preferred_element_type=jnp.float32)

    mixed = group_sums(out_term, own_rows).astype(jnp.bfloat16)
    grad_down = lax.dot_general(act_all, grad_all, inner, preferred_element_type=jnp.float32)
    grad_down_weight = jnp.where(keep_down, grad_down, jnp.float32(0.0)).astype(jnp.bfloat16)
    grad_act = row_sums(act_term, split_rows)
    grads_all = row_gather(swiglu_back(sums, grad_act))
    grad_both = lax.dot_general(x_all, grads_all, inner, preferred_element_type=jnp.float32)
    width = grad_both.shape[1] // 2
    grad_gate_weight = jnp.where(keep_gate, grad_both[:, :width], jnp.float32(0.0)).astype(
        jnp.bfloat16
    )
    grad_up_weight = jnp.where(keep_up, grad_both[:, width:], jnp.float32(0.0)).astype(jnp.bfloat16)

    def input_term(start, count):
        return lax.dot_general(grads_all, w_both, outer, preferred_element_type=jnp.float32)

    grad_tokens = group_sums(input_term, own_rows).astype(jnp.bfloat16)
    return (mixed, grad_tokens, grad_gate_weight, grad_up_weight, grad_down_weight)


def solution(mesh):
    return jax.shard_map(
        local,
        mesh=mesh,
        in_specs=(
            P(("col", "depth"), "row"),
            P("row", ("col", "depth")),
            P("row", ("col", "depth")),
            P(("col", "depth"), "row"),
            P("row", ("col", "depth")),
            P("row", ("col", "depth")),
            P(("col", "depth"), "row"),
            P(("col", "depth"), "row"),
        ),
        out_specs=(
            P(("col", "depth"), "row"),
            P(("col", "depth"), "row"),
            P("row", ("col", "depth")),
            P("row", ("col", "depth")),
            P(("col", "depth"), "row"),
        ),
        check_vma=False,
    )
```

```python
import jax
import jax.numpy as jnp
from jax import lax
from jax.sharding import PartitionSpec as P

BLK = 128
CHUNKS = 2
GROUP = ("col", "depth")


def expand(mask):
    return jnp.repeat(jnp.repeat(mask, BLK, axis=0), BLK, axis=1) > 0


def swiglu(sums):
    width = sums.shape[1] // 2
    gate = sums[:, :width]
    up = sums[:, width:]
    sig = jax.nn.sigmoid(gate)
    return (gate * sig * up).astype(jnp.bfloat16)


def swiglu_back(sums, grad_act):
    width = sums.shape[1] // 2
    gate = sums[:, :width]
    up = sums[:, width:]
    sig = jax.nn.sigmoid(gate)
    grad_gate = grad_act * up * sig * (1.0 + gate * (1.0 - sig))
    grad_up = grad_act * gate * sig
    return jnp.concatenate([grad_gate, grad_up], axis=1).astype(jnp.bfloat16)


def row_sums(full):
    return lax.psum_scatter(full, "row", scatter_dimension=0, tiled=True)


def row_gather(block):
    return lax.all_gather(block, "row", axis=0, tiled=True)


def group_sums(full):
    parts = lax.axis_size(GROUP)
    rows = full.shape[0] // parts
    pieces = lax.all_to_all(
        full.astype(jnp.bfloat16).reshape((parts, rows) + full.shape[1:]), GROUP, 0, 0
    )
    return jnp.sum(pieces.astype(jnp.float32), axis=0)


def group_gather(block):
    parts = lax.axis_size(GROUP)
    copies = jnp.broadcast_to(block[None], (parts,) + block.shape)
    pieces = lax.all_to_all(copies, GROUP, 0, 0)
    return pieces.reshape((parts * block.shape[0],) + block.shape[1:])


def local(tokens, gate_weight, up_weight, down_weight, gate_mask, up_mask, down_mask, grad_out):
    zero_value = jnp.zeros((), jnp.bfloat16)
    keep_gate = expand(gate_mask)
    keep_up = expand(up_mask)
    keep_down = expand(down_mask)
    w_both = jnp.concatenate(
        [jnp.where(keep_gate, gate_weight, zero_value), jnp.where(keep_up, up_weight, zero_value)],
        axis=1,
    )
    w_down = jnp.where(keep_down, down_weight, zero_value)
    inner = (((0,), (0,)), ((), ()))
    outer = (((1,), (1,)), ((), ()))
    step = tokens.shape[0] // CHUNKS

    mixed_parts, input_parts = [], []
    grad_down = None
    grad_both = None
    for h in range(CHUNKS):
        grad_h = group_gather(grad_out[h * step : (h + 1) * step])
        x_h = group_gather(tokens[h * step : (h + 1) * step])
        grad_act = row_sums(lax.dot_general(grad_h, w_down, outer, preferred_element_type=jnp.float32))
        sums = row_sums(jnp.dot(x_h, w_both, preferred_element_type=jnp.float32))
        act_all = row_gather(swiglu(sums))
        grads_all = row_gather(swiglu_back(sums, grad_act))
        mixed_parts.append(group_sums(jnp.dot(act_all, w_down, preferred_element_type=jnp.float32)))
        down_term = lax.dot_general(act_all, grad_h, inner, preferred_element_type=jnp.float32)
        grad_down = down_term if grad_down is None else grad_down + down_term
        input_parts.append(
            group_sums(lax.dot_general(grads_all, w_both, outer, preferred_element_type=jnp.float32))
        )
        both_term = lax.dot_general(x_h, grads_all, inner, preferred_element_type=jnp.float32)
        grad_both = both_term if grad_both is None else grad_both + both_term

    mixed = jnp.concatenate(mixed_parts, axis=0).astype(jnp.bfloat16)
    grad_tokens = jnp.concatenate(input_parts, axis=0).astype(jnp.bfloat16)
    grad_down_weight = jnp.where(keep_down, grad_down, jnp.float32(0.0)).astype(jnp.bfloat16)
    width = grad_both.shape[1] // 2
    grad_gate_weight = jnp.where(keep_gate, grad_both[:, :width], jnp.float32(0.0)).astype(
        jnp.bfloat16
    )
    grad_up_weight = jnp.where(keep_up, grad_both[:, width:], jnp.float32(0.0)).astype(jnp.bfloat16)
    return (mixed, grad_tokens, grad_gate_weight, grad_up_weight, grad_down_weight)


def solution(mesh):
    return jax.shard_map(
        local,
        mesh=mesh,
        in_specs=(
            P(GROUP, "row"),
            P("row", GROUP),
            P("row", GROUP),
            P(GROUP, "row"),
            P("row", GROUP),
            P("row", GROUP),
            P(GROUP, "row"),
            P(GROUP, "row"),
        ),
        out_specs=(
            P(GROUP, "row"),
            P(GROUP, "row"),
            P("row", GROUP),
            P("row", GROUP),
            P(GROUP, "row"),
        ),
        check_vma=False,
    )
```

```python
import jax
import jax.numpy as jnp
from jax import lax
from jax.sharding import PartitionSpec as P

BLK = 128


def expand(mask):
    return jnp.repeat(jnp.repeat(mask, BLK, axis=0), BLK, axis=1) > 0


def swiglu(sums):
    width = sums.shape[1] // 2
    gate = sums[:, :width]
    up = sums[:, width:]
    sig = jax.nn.sigmoid(gate)
    return (gate * sig * up).astype(jnp.bfloat16)


def swiglu_back(sums, grad_act):
    width = sums.shape[1] // 2
    gate = sums[:, :width]
    up = sums[:, width:]
    sig = jax.nn.sigmoid(gate)
    grad_gate = grad_act * up * sig * (1.0 + gate * (1.0 - sig))
    grad_up = grad_act * gate * sig
    return jnp.concatenate([grad_gate, grad_up], axis=1).astype(jnp.bfloat16)


def row_sums(term, rows):
    return lax.psum_scatter(
        term(jnp.int32(0), lax.axis_size("row") * rows), "row", scatter_dimension=0, tiled=True
    )


def row_gather(block):
    return lax.all_gather(block, "row", axis=0, tiled=True)


def group_sums(term, rows):
    parts = lax.axis_size(("col", "depth"))
    full = term(jnp.int32(0), rows * parts).astype(jnp.bfloat16)
    pieces = lax.all_to_all(full.reshape((parts, rows) + full.shape[1:]), ("col", "depth"), 0, 0)
    return jnp.sum(pieces.astype(jnp.float32), axis=0)


def group_gather(block):
    parts = lax.axis_size(("col", "depth"))
    copies = jnp.broadcast_to(block[None], (parts,) + block.shape)
    pieces = lax.all_to_all(copies, ("col", "depth"), 0, 0)
    return pieces.reshape((parts * block.shape[0],) + block.shape[1:])


def local(tokens, gate_weight, up_weight, down_weight, gate_mask, up_mask, down_mask, grad_out):
    zero_value = jnp.zeros((), jnp.bfloat16)
    keep_gate = expand(gate_mask)
    keep_up = expand(up_mask)
    keep_down = expand(down_mask)
    w_both = jnp.concatenate(
        [jnp.where(keep_gate, gate_weight, zero_value), jnp.where(keep_up, up_weight, zero_value)],
        axis=1,
    )
    w_down = jnp.where(keep_down, down_weight, zero_value)
    x_all = group_gather(tokens)
    total = x_all.shape[0]
    split_rows = total // lax.axis_size("row")
    own_rows = tokens.shape[0]
    inner = (((0,), (0,)), ((), ()))
    outer = (((1,), (1,)), ((), ()))

    def hidden_term(start, count):
        return jnp.dot(x_all, w_both, preferred_element_type=jnp.float32)

    sums = row_sums(hidden_term, split_rows)
    act_all = row_gather(swiglu(sums))

    def out_term(start, count):
        return jnp.dot(act_all, w_down, preferred_element_type=jnp.float32)

    mixed = group_sums(out_term, own_rows).astype(jnp.bfloat16)
    grad_all = group_gather(grad_out)
    grad_down = lax.dot_general(act_all, grad_all, inner, preferred_element_type=jnp.float32)
    grad_down_weight = jnp.where(keep_down, grad_down, jnp.float32(0.0)).astype(jnp.bfloat16)

    def act_term(start, count):
        return lax.dot_general(grad_all, w_down, outer, preferred_element_type=jnp.float32)

    grad_act = row_sums(act_term, split_rows)
    held_sums, grad_act = lax.optimization_barrier((sums, grad_act))
    grads_all = row_gather(swiglu_back(held_sums, grad_act))
    grad_both = lax.dot_general(x_all, grads_all, inner, preferred_element_type=jnp.float32)
    width = grad_both.shape[1] // 2
    grad_gate_weight = jnp.where(keep_gate, grad_both[:, :width], jnp.float32(0.0)).astype(
        jnp.bfloat16
    )
    grad_up_weight = jnp.where(keep_up, grad_both[:, width:], jnp.float32(0.0)).astype(jnp.bfloat16)

    def input_term(start, count):
        return lax.dot_general(grads_all, w_both, outer, preferred_element_type=jnp.float32)

    grad_tokens = group_sums(input_term, own_rows).astype(jnp.bfloat16)
    return (mixed, grad_tokens, grad_gate_weight, grad_up_weight, grad_down_weight)


def solution(mesh):
    return jax.shard_map(
        local,
        mesh=mesh,
        in_specs=(
            P(("col", "depth"), "row"),
            P("row", ("col", "depth")),
            P("row", ("col", "depth")),
            P(("col", "depth"), "row"),
            P("row", ("col", "depth")),
            P("row", ("col", "depth")),
            P(("col", "depth"), "row"),
            P(("col", "depth"), "row"),
        ),
        out_specs=(
            P(("col", "depth"), "row"),
            P(("col", "depth"), "row"),
            P("row", ("col", "depth")),
            P("row", ("col", "depth")),
            P(("col", "depth"), "row"),
        ),
        check_vma=False,
    )
```

```python
import jax
import jax.numpy as jnp
from jax import lax
from jax.sharding import PartitionSpec as P

BLK = 128


def expand(mask):
    return jnp.repeat(jnp.repeat(mask, BLK, axis=0), BLK, axis=1) > 0


def swiglu(sums):
    width = sums.shape[1] // 2
    gate = sums[:, :width]
    up = sums[:, width:]
    sig = jax.nn.sigmoid(gate)
    return (gate * sig * up).astype(jnp.bfloat16)


def swiglu_back(sums, grad_act):
    width = sums.shape[1] // 2
    gate = sums[:, :width]
    up = sums[:, width:]
    sig = jax.nn.sigmoid(gate)
    grad_gate = grad_act * up * sig * (1.0 + gate * (1.0 - sig))
    grad_up = grad_act * gate * sig
    return jnp.concatenate([grad_gate, grad_up], axis=1).astype(jnp.bfloat16)


def row_sums(term, rows):
    return lax.psum_scatter(
        term(jnp.int32(0), lax.axis_size("row") * rows), "row", scatter_dimension=0, tiled=True
    )


def row_gather(block):
    return lax.all_gather(block, "row", axis=0, tiled=True)


def row_gather_direct(block):
    parts = lax.axis_size("row")
    copies = jnp.broadcast_to(block[None], (parts,) + block.shape)
    pieces = lax.all_to_all(copies, "row", 0, 0)
    return pieces.reshape((parts * block.shape[0],) + block.shape[1:])


def group_sums(term, rows):
    parts = lax.axis_size(("col", "depth"))
    full = term(jnp.int32(0), rows * parts).astype(jnp.bfloat16)
    pieces = lax.all_to_all(full.reshape((parts, rows) + full.shape[1:]), ("col", "depth"), 0, 0)
    return jnp.sum(pieces.astype(jnp.float32), axis=0)


def group_gather(block):
    parts = lax.axis_size(("col", "depth"))
    copies = jnp.broadcast_to(block[None], (parts,) + block.shape)
    pieces = lax.all_to_all(copies, ("col", "depth"), 0, 0)
    return pieces.reshape((parts * block.shape[0],) + block.shape[1:])


def local(tokens, gate_weight, up_weight, down_weight, gate_mask, up_mask, down_mask, grad_out):
    zero_value = jnp.zeros((), jnp.bfloat16)
    keep_gate = expand(gate_mask)
    keep_up = expand(up_mask)
    keep_down = expand(down_mask)
    w_both = jnp.concatenate(
        [jnp.where(keep_gate, gate_weight, zero_value), jnp.where(keep_up, up_weight, zero_value)],
        axis=1,
    )
    w_down = jnp.where(keep_down, down_weight, zero_value)
    x_all = group_gather(tokens)
    split_rows = x_all.shape[0] // lax.axis_size("row")
    own_rows = tokens.shape[0]
    inner = (((0,), (0,)), ((), ()))
    outer = (((1,), (1,)), ((), ()))

    hidden = jnp.dot(x_all, w_both, preferred_element_type=jnp.float32)
    sums = row_sums(lambda start, count: hidden, split_rows)
    grad_out, _ = lax.optimization_barrier((grad_out, hidden))
    grad_all = group_gather(grad_out)
    act_all = row_gather_direct(swiglu(sums))

    def out_term(start, count):
        return jnp.dot(act_all, w_down, preferred_element_type=jnp.float32)

    mixed = group_sums(out_term, own_rows).astype(jnp.bfloat16)
    grad_down = lax.dot_general(act_all, grad_all, inner, preferred_element_type=jnp.float32)
    grad_down_weight = jnp.where(keep_down, grad_down, jnp.float32(0.0)).astype(jnp.bfloat16)

    def act_term(start, count):
        return lax.dot_general(grad_all, w_down, outer, preferred_element_type=jnp.float32)

    grad_act = row_sums(act_term, split_rows)
    held_sums, grad_act, _ = lax.optimization_barrier((sums, grad_act, act_all))
    grads_all = row_gather(swiglu_back(held_sums, grad_act))
    grad_both = lax.dot_general(x_all, grads_all, inner, preferred_element_type=jnp.float32)
    width = grad_both.shape[1] // 2
    grad_gate_weight = jnp.where(keep_gate, grad_both[:, :width], jnp.float32(0.0)).astype(
        jnp.bfloat16
    )
    grad_up_weight = jnp.where(keep_up, grad_both[:, width:], jnp.float32(0.0)).astype(jnp.bfloat16)

    def input_term(start, count):
        return lax.dot_general(grads_all, w_both, outer, preferred_element_type=jnp.float32)

    grad_tokens = group_sums(input_term, own_rows).astype(jnp.bfloat16)
    return (mixed, grad_tokens, grad_gate_weight, grad_up_weight, grad_down_weight)


def solution(mesh):
    return jax.shard_map(
        local,
        mesh=mesh,
        in_specs=(
            P(("col", "depth"), "row"),
            P("row", ("col", "depth")),
            P("row", ("col", "depth")),
            P(("col", "depth"), "row"),
            P("row", ("col", "depth")),
            P("row", ("col", "depth")),
            P(("col", "depth"), "row"),
            P(("col", "depth"), "row"),
        ),
        out_specs=(
            P(("col", "depth"), "row"),
            P(("col", "depth"), "row"),
            P("row", ("col", "depth")),
            P("row", ("col", "depth")),
            P(("col", "depth"), "row"),
        ),
        check_vma=False,
    )
```

```python
import jax
import jax.numpy as jnp
from jax import lax
from jax.sharding import PartitionSpec as P

BLK = 128


def expand(mask):
    return jnp.repeat(jnp.repeat(mask, BLK, axis=0), BLK, axis=1) > 0


def swiglu(sums):
    width = sums.shape[1] // 2
    gate = sums[:, :width]
    up = sums[:, width:]
    sig = jax.nn.sigmoid(gate)
    return (gate * sig * up).astype(jnp.bfloat16)


def swiglu_back(sums, grad_act):
    width = sums.shape[1] // 2
    gate = sums[:, :width]
    up = sums[:, width:]
    sig = jax.nn.sigmoid(gate)
    grad_gate = grad_act * up * sig * (1.0 + gate * (1.0 - sig))
    grad_up = grad_act * gate * sig
    return jnp.concatenate([grad_gate, grad_up], axis=1).astype(jnp.bfloat16)


def row_sums(term, rows):
    return lax.psum_scatter(
        term(jnp.int32(0), lax.axis_size("row") * rows), "row", scatter_dimension=0, tiled=True
    )


def row_gather(block):
    return lax.all_gather(block, "row", axis=0, tiled=True)


def row_sums_direct(full):
    parts = lax.axis_size("row")
    rows = full.shape[0] // parts
    pieces = lax.all_to_all(
        full.astype(jnp.bfloat16).reshape((parts, rows) + full.shape[1:]), "row", 0, 0
    )
    return jnp.sum(pieces.astype(jnp.float32), axis=0)


def row_gather_direct(block):
    parts = lax.axis_size("row")
    copies = jnp.broadcast_to(block[None], (parts,) + block.shape)
    pieces = lax.all_to_all(copies, "row", 0, 0)
    return pieces.reshape((parts * block.shape[0],) + block.shape[1:])


def group_sums(term, rows):
    parts = lax.axis_size(("col", "depth"))
    full = term(jnp.int32(0), rows * parts).astype(jnp.bfloat16)
    pieces = lax.all_to_all(full.reshape((parts, rows) + full.shape[1:]), ("col", "depth"), 0, 0)
    return jnp.sum(pieces.astype(jnp.float32), axis=0)


def group_gather(block):
    parts = lax.axis_size(("col", "depth"))
    copies = jnp.broadcast_to(block[None], (parts,) + block.shape)
    pieces = lax.all_to_all(copies, ("col", "depth"), 0, 0)
    return pieces.reshape((parts * block.shape[0],) + block.shape[1:])


def local(tokens, gate_weight, up_weight, down_weight, gate_mask, up_mask, down_mask, grad_out):
    zero_value = jnp.zeros((), jnp.bfloat16)
    keep_gate = expand(gate_mask)
    keep_up = expand(up_mask)
    keep_down = expand(down_mask)
    w_both = jnp.concatenate(
        [jnp.where(keep_gate, gate_weight, zero_value), jnp.where(keep_up, up_weight, zero_value)],
        axis=1,
    )
    w_down = jnp.where(keep_down, down_weight, zero_value)
    x_all = group_gather(tokens)
    split_rows = x_all.shape[0] // lax.axis_size("row")
    own_rows = tokens.shape[0]
    inner = (((0,), (0,)), ((), ()))
    outer = (((1,), (1,)), ((), ()))

    hidden = jnp.dot(x_all, w_both, preferred_element_type=jnp.float32)
    sums = row_sums(lambda start, count: hidden, split_rows)
    grad_out, _ = lax.optimization_barrier((grad_out, hidden))
    grad_all = group_gather(grad_out)
    act_all = row_gather(swiglu(sums))

    def out_term(start, count):
        return jnp.dot(act_all, w_down, preferred_element_type=jnp.float32)

    mixed = group_sums(out_term, own_rows).astype(jnp.bfloat16)
    grad_down = lax.dot_general(act_all, grad_all, inner, preferred_element_type=jnp.float32)
    grad_down_weight = jnp.where(keep_down, grad_down, jnp.float32(0.0)).astype(jnp.bfloat16)

    def act_term(start, count):
        return lax.dot_general(grad_all, w_down, outer, preferred_element_type=jnp.float32)

    grad_act = row_sums_direct(act_term(0, split_rows))
    held_sums, grad_act, _ = lax.optimization_barrier((sums, grad_act, act_all))
    grads_all = row_gather(swiglu_back(held_sums, grad_act))
    grad_both = lax.dot_general(x_all, grads_all, inner, preferred_element_type=jnp.float32)
    width = grad_both.shape[1] // 2
    grad_gate_weight = jnp.where(keep_gate, grad_both[:, :width], jnp.float32(0.0)).astype(
        jnp.bfloat16
    )
    grad_up_weight = jnp.where(keep_up, grad_both[:, width:], jnp.float32(0.0)).astype(jnp.bfloat16)

    def input_term(start, count):
        return lax.dot_general(grads_all, w_both, outer, preferred_element_type=jnp.float32)

    grad_tokens = group_sums(input_term, own_rows).astype(jnp.bfloat16)
    return (mixed, grad_tokens, grad_gate_weight, grad_up_weight, grad_down_weight)


def solution(mesh):
    return jax.shard_map(
        local,
        mesh=mesh,
        in_specs=(
            P(("col", "depth"), "row"),
            P("row", ("col", "depth")),
            P("row", ("col", "depth")),
            P(("col", "depth"), "row"),
            P("row", ("col", "depth")),
            P("row", ("col", "depth")),
            P(("col", "depth"), "row"),
            P(("col", "depth"), "row"),
        ),
        out_specs=(
            P(("col", "depth"), "row"),
            P(("col", "depth"), "row"),
            P("row", ("col", "depth")),
            P("row", ("col", "depth")),
            P(("col", "depth"), "row"),
        ),
        check_vma=False,
    )
```

```python
import jax
import jax.numpy as jnp
from jax import lax
from jax.sharding import PartitionSpec as P

BLK = 128


def expand(mask):
    return jnp.repeat(jnp.repeat(mask, BLK, axis=0), BLK, axis=1) > 0


def swiglu(sums):
    width = sums.shape[1] // 2
    gate = sums[:, :width]
    up = sums[:, width:]
    sig = jax.nn.sigmoid(gate)
    return (gate * sig * up).astype(jnp.bfloat16)


def swiglu_back(sums, grad_act):
    width = sums.shape[1] // 2
    gate = sums[:, :width]
    up = sums[:, width:]
    sig = jax.nn.sigmoid(gate)
    grad_gate = grad_act * up * sig * (1.0 + gate * (1.0 - sig))
    grad_up = grad_act * gate * sig
    return jnp.concatenate([grad_gate, grad_up], axis=1).astype(jnp.bfloat16)


def row_sums(term, rows):
    return lax.psum_scatter(
        term(jnp.int32(0), lax.axis_size("row") * rows), "row", scatter_dimension=0, tiled=True
    )


def row_gather(block):
    return lax.all_gather(block, "row", axis=0, tiled=True)


def row_sums_direct(full):
    parts = lax.axis_size("row")
    rows = full.shape[0] // parts
    pieces = lax.all_to_all(
        full.astype(jnp.bfloat16).reshape((parts, rows) + full.shape[1:]), "row", 0, 0
    )
    return jnp.sum(pieces.astype(jnp.float32), axis=0)


def row_gather_direct(block):
    parts = lax.axis_size("row")
    copies = jnp.broadcast_to(block[None], (parts,) + block.shape)
    pieces = lax.all_to_all(copies, "row", 0, 0)
    return pieces.reshape((parts * block.shape[0],) + block.shape[1:])


def group_sums(term, rows):
    parts = lax.axis_size(("col", "depth"))
    full = term(jnp.int32(0), rows * parts).astype(jnp.bfloat16)
    pieces = lax.all_to_all(full.reshape((parts, rows) + full.shape[1:]), ("col", "depth"), 0, 0)
    return jnp.sum(pieces.astype(jnp.float32), axis=0)


def group_gather(block):
    parts = lax.axis_size(("col", "depth"))
    copies = jnp.broadcast_to(block[None], (parts,) + block.shape)
    pieces = lax.all_to_all(copies, ("col", "depth"), 0, 0)
    return pieces.reshape((parts * block.shape[0],) + block.shape[1:])


def local(tokens, gate_weight, up_weight, down_weight, gate_mask, up_mask, down_mask, grad_out):
    zero_value = jnp.zeros((), jnp.bfloat16)
    keep_gate = expand(gate_mask)
    keep_up = expand(up_mask)
    keep_down = expand(down_mask)
    w_both = jnp.concatenate(
        [jnp.where(keep_gate, gate_weight, zero_value), jnp.where(keep_up, up_weight, zero_value)],
        axis=1,
    )
    w_down = jnp.where(keep_down, down_weight, zero_value)
    x_all = group_gather(tokens)
    split_rows = x_all.shape[0] // lax.axis_size("row")
    own_rows = tokens.shape[0]
    inner = (((0,), (0,)), ((), ()))
    outer = (((1,), (1,)), ((), ()))

    hidden = jnp.dot(x_all, w_both, preferred_element_type=jnp.float32)
    sums = row_sums(lambda start, count: hidden, split_rows)
    grad_out, _ = lax.optimization_barrier((grad_out, hidden))
    grad_all = group_gather(grad_out)
    act_partial = lax.dot_general(grad_all, w_down, outer, preferred_element_type=jnp.float32)
    act_sums, act_partial = lax.optimization_barrier((sums, act_partial))
    act_all = row_gather(swiglu(act_sums))

    def out_term(start, count):
        return jnp.dot(act_all, w_down, preferred_element_type=jnp.float32)

    mixed = group_sums(out_term, own_rows).astype(jnp.bfloat16)
    grad_down = lax.dot_general(act_all, grad_all, inner, preferred_element_type=jnp.float32)
    grad_down_weight = jnp.where(keep_down, grad_down, jnp.float32(0.0)).astype(jnp.bfloat16)

    grad_act = row_sums_direct(act_partial)
    held_sums, grad_act, _ = lax.optimization_barrier((sums, grad_act, act_all))
    grads_all = row_gather(swiglu_back(held_sums, grad_act))
    grad_both = lax.dot_general(x_all, grads_all, inner, preferred_element_type=jnp.float32)
    width = grad_both.shape[1] // 2
    grad_gate_weight = jnp.where(keep_gate, grad_both[:, :width], jnp.float32(0.0)).astype(
        jnp.bfloat16
    )
    grad_up_weight = jnp.where(keep_up, grad_both[:, width:], jnp.float32(0.0)).astype(jnp.bfloat16)

    def input_term(start, count):
        return lax.dot_general(grads_all, w_both, outer, preferred_element_type=jnp.float32)

    grad_tokens = group_sums(input_term, own_rows).astype(jnp.bfloat16)
    return (mixed, grad_tokens, grad_gate_weight, grad_up_weight, grad_down_weight)


def solution(mesh):
    return jax.shard_map(
        local,
        mesh=mesh,
        in_specs=(
            P(("col", "depth"), "row"),
            P("row", ("col", "depth")),
            P("row", ("col", "depth")),
            P(("col", "depth"), "row"),
            P("row", ("col", "depth")),
            P("row", ("col", "depth")),
            P(("col", "depth"), "row"),
            P(("col", "depth"), "row"),
        ),
        out_specs=(
            P(("col", "depth"), "row"),
            P(("col", "depth"), "row"),
            P("row", ("col", "depth")),
            P("row", ("col", "depth")),
            P(("col", "depth"), "row"),
        ),
        check_vma=False,
    )
```

```python
import jax
import jax.numpy as jnp
from jax import lax
from jax.sharding import PartitionSpec as P

BLK = 128
GROUP = ("col", "depth")


def expand(mask):
    return jnp.repeat(jnp.repeat(mask, BLK, axis=0), BLK, axis=1) > 0


def swiglu(sums):
    width = sums.shape[1] // 2
    gate = sums[:, :width]
    up = sums[:, width:]
    sig = jax.nn.sigmoid(gate)
    return (gate * sig * up).astype(jnp.bfloat16)


def swiglu_back(sums, grad_act):
    width = sums.shape[1] // 2
    gate = sums[:, :width]
    up = sums[:, width:]
    sig = jax.nn.sigmoid(gate)
    grad_gate = grad_act * up * sig * (1.0 + gate * (1.0 - sig))
    grad_up = grad_act * gate * sig
    return jnp.concatenate([grad_gate, grad_up], axis=1).astype(jnp.bfloat16)


def row_sums(term, rows):
    return lax.psum_scatter(
        term(jnp.int32(0), lax.axis_size("row") * rows), "row", scatter_dimension=0, tiled=True
    )


def row_gather(block):
    return lax.all_gather(block, "row", axis=0, tiled=True)


def row_sums_direct(full):
    parts = lax.axis_size("row")
    rows = full.shape[0] // parts
    pieces = lax.all_to_all(
        full.astype(jnp.bfloat16).reshape((parts, rows) + full.shape[1:]), "row", 0, 0
    )
    return jnp.sum(pieces.astype(jnp.float32), axis=0)


def row_gather_direct(block):
    parts = lax.axis_size("row")
    copies = jnp.broadcast_to(block[None], (parts,) + block.shape)
    pieces = lax.all_to_all(copies, "row", 0, 0)
    return pieces.reshape((parts * block.shape[0],) + block.shape[1:])


def group_sums(term, rows):
    parts = lax.axis_size(("col", "depth"))
    full = term(jnp.int32(0), rows * parts).astype(jnp.bfloat16)
    pieces = lax.all_to_all(full.reshape((parts, rows) + full.shape[1:]), ("col", "depth"), 0, 0)
    return jnp.sum(pieces.astype(jnp.float32), axis=0)


def group_gather(block):
    parts = lax.axis_size(("col", "depth"))
    copies = jnp.broadcast_to(block[None], (parts,) + block.shape)
    pieces = lax.all_to_all(copies, ("col", "depth"), 0, 0)
    return pieces.reshape((parts * block.shape[0],) + block.shape[1:])


def local(tokens, gate_weight, up_weight, down_weight, gate_mask, up_mask, down_mask, grad_out):
    zero_value = jnp.zeros((), jnp.bfloat16)
    keep_gate = expand(gate_mask)
    keep_up = expand(up_mask)
    keep_down = expand(down_mask)
    w_both = jnp.concatenate(
        [jnp.where(keep_gate, gate_weight, zero_value), jnp.where(keep_up, up_weight, zero_value)],
        axis=1,
    )
    w_down = jnp.where(keep_down, down_weight, zero_value)
    x_all = group_gather(tokens)
    split_rows = x_all.shape[0] // lax.axis_size("row")
    own_rows = tokens.shape[0]
    inner = (((0,), (0,)), ((), ()))
    outer = (((1,), (1,)), ((), ()))

    hidden = jnp.dot(x_all, w_both, preferred_element_type=jnp.float32)
    sums = row_sums(lambda start, count: hidden, split_rows)
    grad_all = lax.all_gather(grad_out, GROUP, axis=0, tiled=True)
    act_partial = lax.dot_general(grad_all, w_down, outer, preferred_element_type=jnp.float32)
    grad_act = row_sums_direct(act_partial)
    act_sums, grad_act = lax.optimization_barrier((sums, grad_act))
    act_all = row_gather(swiglu(act_sums))

    def out_term(start, count):
        return jnp.dot(act_all, w_down, preferred_element_type=jnp.float32)

    mixed = group_sums(out_term, own_rows).astype(jnp.bfloat16)
    grad_down = lax.dot_general(act_all, grad_all, inner, preferred_element_type=jnp.float32)
    grad_down_weight = jnp.where(keep_down, grad_down, jnp.float32(0.0)).astype(jnp.bfloat16)

    held_sums, grad_act, _ = lax.optimization_barrier((act_sums, grad_act, act_all))
    grads_all = row_gather(swiglu_back(held_sums, grad_act))
    grad_both = lax.dot_general(x_all, grads_all, inner, preferred_element_type=jnp.float32)
    width = grad_both.shape[1] // 2
    grad_gate_weight = jnp.where(keep_gate, grad_both[:, :width], jnp.float32(0.0)).astype(
        jnp.bfloat16
    )
    grad_up_weight = jnp.where(keep_up, grad_both[:, width:], jnp.float32(0.0)).astype(jnp.bfloat16)

    def input_term(start, count):
        return lax.dot_general(grads_all, w_both, outer, preferred_element_type=jnp.float32)

    grad_tokens = group_sums(input_term, own_rows).astype(jnp.bfloat16)
    return (mixed, grad_tokens, grad_gate_weight, grad_up_weight, grad_down_weight)


def solution(mesh):
    return jax.shard_map(
        local,
        mesh=mesh,
        in_specs=(
            P(("col", "depth"), "row"),
            P("row", ("col", "depth")),
            P("row", ("col", "depth")),
            P(("col", "depth"), "row"),
            P("row", ("col", "depth")),
            P("row", ("col", "depth")),
            P(("col", "depth"), "row"),
            P(("col", "depth"), "row"),
        ),
        out_specs=(
            P(("col", "depth"), "row"),
            P(("col", "depth"), "row"),
            P("row", ("col", "depth")),
            P("row", ("col", "depth")),
            P(("col", "depth"), "row"),
        ),
        check_vma=False,
    )
```

```python
import jax
import jax.numpy as jnp
from jax import lax
from jax.sharding import PartitionSpec as P

BLK = 128


def expand(mask):
    return jnp.repeat(jnp.repeat(mask, BLK, axis=0), BLK, axis=1) > 0


def swiglu(sums):
    width = sums.shape[1] // 2
    gate = sums[:, :width]
    up = sums[:, width:]
    sig = jax.nn.sigmoid(gate)
    return (gate * sig * up).astype(jnp.bfloat16)


def swiglu_back(sums, grad_act):
    width = sums.shape[1] // 2
    gate = sums[:, :width]
    up = sums[:, width:]
    sig = jax.nn.sigmoid(gate)
    grad_gate = grad_act * up * sig * (1.0 + gate * (1.0 - sig))
    grad_up = grad_act * gate * sig
    return jnp.concatenate([grad_gate, grad_up], axis=1).astype(jnp.bfloat16)


def row_sums(term, rows):
    return lax.psum_scatter(
        term(jnp.int32(0), lax.axis_size("row") * rows), "row", scatter_dimension=0, tiled=True
    )


def row_gather(block):
    return lax.all_gather(block, "row", axis=0, tiled=True)


def row_sums_direct(full):
    parts = lax.axis_size("row")
    rows = full.shape[0] // parts
    pieces = lax.all_to_all(
        full.astype(jnp.bfloat16).reshape((parts, rows) + full.shape[1:]), "row", 0, 0
    )
    return jnp.sum(pieces.astype(jnp.float32), axis=0)


def row_sums_paired(full):
    parts = lax.axis_size("row")
    chips = parts // 2
    rows = full.shape[0] // parts
    member = lax.axis_index("row")
    core = member % 2
    chip = member // 2
    blocks = full.reshape((chips, 2, rows) + full.shape[1:])
    give = jnp.take(blocks, 1 - core, axis=1)
    keep = jnp.take(blocks, core, axis=1)
    pair = keep + lax.ppermute(give, "row", [(i, i ^ 1) for i in range(parts)])
    sent = pair.astype(jnp.bfloat16)
    total = jnp.take(pair, chip, axis=0)
    for hop in range(1, chips):
        piece = jnp.take(sent, (chip + hop) % chips, axis=0)
        moved = lax.ppermute(piece, "row", [(i, (i + 2 * hop) % parts) for i in range(parts)])
        total = total + moved.astype(jnp.float32)
    return total


def row_gather_direct(block):
    parts = lax.axis_size("row")
    copies = jnp.broadcast_to(block[None], (parts,) + block.shape)
    pieces = lax.all_to_all(copies, "row", 0, 0)
    return pieces.reshape((parts * block.shape[0],) + block.shape[1:])


def group_sums(term, rows):
    parts = lax.axis_size(("col", "depth"))
    full = term(jnp.int32(0), rows * parts).astype(jnp.bfloat16)
    pieces = lax.all_to_all(full.reshape((parts, rows) + full.shape[1:]), ("col", "depth"), 0, 0)
    return jnp.sum(pieces.astype(jnp.float32), axis=0)


def group_gather(block):
    parts = lax.axis_size(("col", "depth"))
    copies = jnp.broadcast_to(block[None], (parts,) + block.shape)
    pieces = lax.all_to_all(copies, ("col", "depth"), 0, 0)
    return pieces.reshape((parts * block.shape[0],) + block.shape[1:])


def local(tokens, gate_weight, up_weight, down_weight, gate_mask, up_mask, down_mask, grad_out):
    zero_value = jnp.zeros((), jnp.bfloat16)
    keep_gate = expand(gate_mask)
    keep_up = expand(up_mask)
    keep_down = expand(down_mask)
    w_both = jnp.concatenate(
        [jnp.where(keep_gate, gate_weight, zero_value), jnp.where(keep_up, up_weight, zero_value)],
        axis=1,
    )
    w_down = jnp.where(keep_down, down_weight, zero_value)
    x_all = group_gather(tokens)
    split_rows = x_all.shape[0] // lax.axis_size("row")
    own_rows = tokens.shape[0]
    inner = (((0,), (0,)), ((), ()))
    outer = (((1,), (1,)), ((), ()))

    hidden = jnp.dot(x_all, w_both, preferred_element_type=jnp.float32)
    sums = row_sums(lambda start, count: hidden, split_rows)
    grad_out, _ = lax.optimization_barrier((grad_out, hidden))
    grad_all = group_gather(grad_out)
    act_partial = lax.dot_general(grad_all, w_down, outer, preferred_element_type=jnp.float32)
    act_sums, act_partial = lax.optimization_barrier((sums, act_partial))
    act_all = row_gather(swiglu(act_sums))

    def out_term(start, count):
        return jnp.dot(act_all, w_down, preferred_element_type=jnp.float32)

    mixed = group_sums(out_term, own_rows).astype(jnp.bfloat16)
    grad_down = lax.dot_general(act_all, grad_all, inner, preferred_element_type=jnp.float32)
    grad_down_weight = jnp.where(keep_down, grad_down, jnp.float32(0.0)).astype(jnp.bfloat16)

    grad_act = row_sums_paired(act_partial)
    held_sums, grad_act, _ = lax.optimization_barrier((sums, grad_act, act_all))
    grads_all = row_gather(swiglu_back(held_sums, grad_act))
    grad_both = lax.dot_general(x_all, grads_all, inner, preferred_element_type=jnp.float32)
    width = grad_both.shape[1] // 2
    grad_gate_weight = jnp.where(keep_gate, grad_both[:, :width], jnp.float32(0.0)).astype(
        jnp.bfloat16
    )
    grad_up_weight = jnp.where(keep_up, grad_both[:, width:], jnp.float32(0.0)).astype(jnp.bfloat16)

    def input_term(start, count):
        return lax.dot_general(grads_all, w_both, outer, preferred_element_type=jnp.float32)

    grad_tokens = group_sums(input_term, own_rows).astype(jnp.bfloat16)
    return (mixed, grad_tokens, grad_gate_weight, grad_up_weight, grad_down_weight)


def solution(mesh):
    return jax.shard_map(
        local,
        mesh=mesh,
        in_specs=(
            P(("col", "depth"), "row"),
            P("row", ("col", "depth")),
            P("row", ("col", "depth")),
            P(("col", "depth"), "row"),
            P("row", ("col", "depth")),
            P("row", ("col", "depth")),
            P(("col", "depth"), "row"),
            P(("col", "depth"), "row"),
        ),
        out_specs=(
            P(("col", "depth"), "row"),
            P(("col", "depth"), "row"),
            P("row", ("col", "depth")),
            P("row", ("col", "depth")),
            P(("col", "depth"), "row"),
        ),
        check_vma=False,
    )
```

```python
import jax
import jax.numpy as jnp
from jax import lax
from jax.sharding import PartitionSpec as P

BLK = 128


def expand(mask):
    return jnp.repeat(jnp.repeat(mask, BLK, axis=0), BLK, axis=1) > 0


def swiglu(sums):
    width = sums.shape[1] // 2
    gate = sums[:, :width]
    up = sums[:, width:]
    sig = jax.nn.sigmoid(gate)
    return (gate * sig * up).astype(jnp.bfloat16)


def swiglu_back(sums, grad_act):
    width = sums.shape[1] // 2
    gate = sums[:, :width]
    up = sums[:, width:]
    sig = jax.nn.sigmoid(gate)
    grad_gate = grad_act * up * sig * (1.0 + gate * (1.0 - sig))
    grad_up = grad_act * gate * sig
    return jnp.concatenate([grad_gate, grad_up], axis=1).astype(jnp.bfloat16)


def row_sums(term, rows):
    return lax.psum_scatter(
        term(jnp.int32(0), lax.axis_size("row") * rows), "row", scatter_dimension=0, tiled=True
    )


def row_gather(block):
    return lax.all_gather(block, "row", axis=0, tiled=True)


def row_sums_direct(full):
    parts = lax.axis_size("row")
    rows = full.shape[0] // parts
    pieces = lax.all_to_all(
        full.astype(jnp.bfloat16).reshape((parts, rows) + full.shape[1:]), "row", 0, 0
    )
    return jnp.sum(pieces.astype(jnp.float32), axis=0)


def row_sums_paired(full):
    parts = lax.axis_size("row")
    chips = parts // 2
    rows = full.shape[0] // parts
    member = lax.axis_index("row")
    core = member % 2
    chip = member // 2
    blocks = full.reshape((chips, 2, rows) + full.shape[1:])
    give = jnp.take(blocks, 1 - core, axis=1)
    keep = jnp.take(blocks, core, axis=1)
    pair = keep + lax.ppermute(give, "row", [(i, i ^ 1) for i in range(parts)])
    sent = pair.astype(jnp.bfloat16)
    total = jnp.take(pair, chip, axis=0)
    for hop in range(1, chips):
        piece = jnp.take(sent, (chip + hop) % chips, axis=0)
        moved = lax.ppermute(piece, "row", [(i, (i + 2 * hop) % parts) for i in range(parts)])
        total = total + moved.astype(jnp.float32)
    return total


def row_gather_direct(block):
    parts = lax.axis_size("row")
    copies = jnp.broadcast_to(block[None], (parts,) + block.shape)
    pieces = lax.all_to_all(copies, "row", 0, 0)
    return pieces.reshape((parts * block.shape[0],) + block.shape[1:])


def group_sums(term, rows):
    parts = lax.axis_size(("col", "depth"))
    full = term(jnp.int32(0), rows * parts).astype(jnp.bfloat16)
    pieces = lax.all_to_all(full.reshape((parts, rows) + full.shape[1:]), ("col", "depth"), 0, 0)
    return jnp.sum(pieces.astype(jnp.float32), axis=0)


def group_gather(block):
    parts = lax.axis_size(("col", "depth"))
    copies = jnp.broadcast_to(block[None], (parts,) + block.shape)
    pieces = lax.all_to_all(copies, ("col", "depth"), 0, 0)
    return pieces.reshape((parts * block.shape[0],) + block.shape[1:])


def local(tokens, gate_weight, up_weight, down_weight, gate_mask, up_mask, down_mask, grad_out):
    zero_value = jnp.zeros((), jnp.bfloat16)
    keep_gate = expand(gate_mask)
    keep_up = expand(up_mask)
    keep_down = expand(down_mask)
    w_both = jnp.concatenate(
        [jnp.where(keep_gate, gate_weight, zero_value), jnp.where(keep_up, up_weight, zero_value)],
        axis=1,
    )
    w_down = jnp.where(keep_down, down_weight, zero_value)
    x_all = group_gather(tokens)
    split_rows = x_all.shape[0] // lax.axis_size("row")
    own_rows = tokens.shape[0]
    inner = (((0,), (0,)), ((), ()))
    outer = (((1,), (1,)), ((), ()))

    half = w_both.shape[1] // 2
    gate_part = jnp.dot(x_all, w_both[:, :half], preferred_element_type=jnp.float32)
    up_part = jnp.dot(x_all, w_both[:, half:], preferred_element_type=jnp.float32)
    gate_sums = row_sums(lambda start, count: gate_part, split_rows)
    grad_out, _, _ = lax.optimization_barrier((grad_out, gate_part, up_part))
    sums = jnp.concatenate([gate_sums, row_sums_paired(up_part)], axis=1)
    grad_all = group_gather(grad_out)
    act_partial = lax.dot_general(grad_all, w_down, outer, preferred_element_type=jnp.float32)
    act_sums, act_partial = lax.optimization_barrier((sums, act_partial))
    act_all = row_gather(swiglu(act_sums))

    def out_term(start, count):
        return jnp.dot(act_all, w_down, preferred_element_type=jnp.float32)

    mixed = group_sums(out_term, own_rows).astype(jnp.bfloat16)
    grad_down = lax.dot_general(act_all, grad_all, inner, preferred_element_type=jnp.float32)
    grad_down_weight = jnp.where(keep_down, grad_down, jnp.float32(0.0)).astype(jnp.bfloat16)

    grad_act = row_sums_paired(act_partial)
    held_sums, grad_act, _ = lax.optimization_barrier((sums, grad_act, act_all))
    grads_all = row_gather(swiglu_back(held_sums, grad_act))
    grad_both = lax.dot_general(x_all, grads_all, inner, preferred_element_type=jnp.float32)
    width = grad_both.shape[1] // 2
    grad_gate_weight = jnp.where(keep_gate, grad_both[:, :width], jnp.float32(0.0)).astype(
        jnp.bfloat16
    )
    grad_up_weight = jnp.where(keep_up, grad_both[:, width:], jnp.float32(0.0)).astype(jnp.bfloat16)

    def input_term(start, count):
        return lax.dot_general(grads_all, w_both, outer, preferred_element_type=jnp.float32)

    grad_tokens = group_sums(input_term, own_rows).astype(jnp.bfloat16)
    return (mixed, grad_tokens, grad_gate_weight, grad_up_weight, grad_down_weight)


def solution(mesh):
    return jax.shard_map(
        local,
        mesh=mesh,
        in_specs=(
            P(("col", "depth"), "row"),
            P("row", ("col", "depth")),
            P("row", ("col", "depth")),
            P(("col", "depth"), "row"),
            P("row", ("col", "depth")),
            P("row", ("col", "depth")),
            P(("col", "depth"), "row"),
            P(("col", "depth"), "row"),
        ),
        out_specs=(
            P(("col", "depth"), "row"),
            P(("col", "depth"), "row"),
            P("row", ("col", "depth")),
            P("row", ("col", "depth")),
            P(("col", "depth"), "row"),
        ),
        check_vma=False,
    )
```

```python
import jax
import jax.numpy as jnp
from jax import lax
from jax.sharding import PartitionSpec as P

BLK = 128


def expand(mask):
    return jnp.repeat(jnp.repeat(mask, BLK, axis=0), BLK, axis=1) > 0


def swiglu(sums):
    width = sums.shape[1] // 2
    gate = sums[:, :width]
    up = sums[:, width:]
    sig = jax.nn.sigmoid(gate)
    return (gate * sig * up).astype(jnp.bfloat16)


def swiglu_back(sums, grad_act):
    width = sums.shape[1] // 2
    gate = sums[:, :width]
    up = sums[:, width:]
    sig = jax.nn.sigmoid(gate)
    grad_gate = grad_act * up * sig * (1.0 + gate * (1.0 - sig))
    grad_up = grad_act * gate * sig
    return jnp.concatenate([grad_gate, grad_up], axis=1).astype(jnp.bfloat16)


def row_sums(term, rows):
    return lax.psum_scatter(
        term(jnp.int32(0), lax.axis_size("row") * rows), "row", scatter_dimension=0, tiled=True
    )


def row_gather(block):
    return lax.all_gather(block, "row", axis=0, tiled=True)


def row_sums_direct(full):
    parts = lax.axis_size("row")
    rows = full.shape[0] // parts
    pieces = lax.all_to_all(
        full.astype(jnp.bfloat16).reshape((parts, rows) + full.shape[1:]), "row", 0, 0
    )
    return jnp.sum(pieces.astype(jnp.float32), axis=0)


def row_sums_paired(full):
    parts = lax.axis_size("row")
    chips = parts // 2
    rows = full.shape[0] // parts
    member = lax.axis_index("row")
    chip = member // 2
    blocks = full.reshape((chips, 2, rows) + full.shape[1:])
    even, odd = blocks[:, 0], blocks[:, 1]
    from_even = lax.ppermute(odd, "row", [(2 * i, 2 * i + 1) for i in range(chips)])
    from_odd = lax.ppermute(even, "row", [(2 * i + 1, 2 * i) for i in range(chips)])
    pair = jnp.where(member % 2 == 0, even + from_odd, odd + from_even)
    sent = pair.astype(jnp.bfloat16)
    total = jnp.take(pair, chip, axis=0)
    for hop in range(1, chips):
        piece = jnp.take(sent, (chip + hop) % chips, axis=0)
        moved = lax.ppermute(piece, "row", [(i, (i + 2 * hop) % parts) for i in range(parts)])
        total = total + moved.astype(jnp.float32)
    return total


def row_gather_direct(block):
    parts = lax.axis_size("row")
    copies = jnp.broadcast_to(block[None], (parts,) + block.shape)
    pieces = lax.all_to_all(copies, "row", 0, 0)
    return pieces.reshape((parts * block.shape[0],) + block.shape[1:])


def group_sums(term, rows):
    parts = lax.axis_size(("col", "depth"))
    full = term(jnp.int32(0), rows * parts).astype(jnp.bfloat16)
    pieces = lax.all_to_all(full.reshape((parts, rows) + full.shape[1:]), ("col", "depth"), 0, 0)
    return jnp.sum(pieces.astype(jnp.float32), axis=0)


def group_gather(block):
    parts = lax.axis_size(("col", "depth"))
    copies = jnp.broadcast_to(block[None], (parts,) + block.shape)
    pieces = lax.all_to_all(copies, ("col", "depth"), 0, 0)
    return pieces.reshape((parts * block.shape[0],) + block.shape[1:])


def local(tokens, gate_weight, up_weight, down_weight, gate_mask, up_mask, down_mask, grad_out):
    zero_value = jnp.zeros((), jnp.bfloat16)
    keep_gate = expand(gate_mask)
    keep_up = expand(up_mask)
    keep_down = expand(down_mask)
    w_both = jnp.concatenate(
        [jnp.where(keep_gate, gate_weight, zero_value), jnp.where(keep_up, up_weight, zero_value)],
        axis=1,
    )
    w_down = jnp.where(keep_down, down_weight, zero_value)
    x_all = group_gather(tokens)
    split_rows = x_all.shape[0] // lax.axis_size("row")
    own_rows = tokens.shape[0]
    inner = (((0,), (0,)), ((), ()))
    outer = (((1,), (1,)), ((), ()))

    hidden = jnp.dot(x_all, w_both, preferred_element_type=jnp.float32)
    sums = row_sums(lambda start, count: hidden, split_rows)
    grad_out, _ = lax.optimization_barrier((grad_out, hidden))
    grad_all = group_gather(grad_out)
    act_partial = lax.dot_general(grad_all, w_down, outer, preferred_element_type=jnp.float32)
    act_sums, act_partial = lax.optimization_barrier((sums, act_partial))
    act_all = row_gather(swiglu(act_sums))

    def out_term(start, count):
        return jnp.dot(act_all, w_down, preferred_element_type=jnp.float32)

    mixed = group_sums(out_term, own_rows).astype(jnp.bfloat16)
    grad_down = lax.dot_general(act_all, grad_all, inner, preferred_element_type=jnp.float32)
    grad_down_weight = jnp.where(keep_down, grad_down, jnp.float32(0.0)).astype(jnp.bfloat16)

    grad_act = row_sums_paired(act_partial)
    held_sums, grad_act, _ = lax.optimization_barrier((sums, grad_act, act_all))
    grads_all = row_gather(swiglu_back(held_sums, grad_act))
    grad_both = lax.dot_general(x_all, grads_all, inner, preferred_element_type=jnp.float32)
    width = grad_both.shape[1] // 2
    grad_gate_weight = jnp.where(keep_gate, grad_both[:, :width], jnp.float32(0.0)).astype(
        jnp.bfloat16
    )
    grad_up_weight = jnp.where(keep_up, grad_both[:, width:], jnp.float32(0.0)).astype(jnp.bfloat16)

    def input_term(start, count):
        return lax.dot_general(grads_all, w_both, outer, preferred_element_type=jnp.float32)

    grad_tokens = group_sums(input_term, own_rows).astype(jnp.bfloat16)
    return (mixed, grad_tokens, grad_gate_weight, grad_up_weight, grad_down_weight)


def solution(mesh):
    return jax.shard_map(
        local,
        mesh=mesh,
        in_specs=(
            P(("col", "depth"), "row"),
            P("row", ("col", "depth")),
            P("row", ("col", "depth")),
            P(("col", "depth"), "row"),
            P("row", ("col", "depth")),
            P("row", ("col", "depth")),
            P(("col", "depth"), "row"),
            P(("col", "depth"), "row"),
        ),
        out_specs=(
            P(("col", "depth"), "row"),
            P(("col", "depth"), "row"),
            P("row", ("col", "depth")),
            P("row", ("col", "depth")),
            P(("col", "depth"), "row"),
        ),
        check_vma=False,
    )
```

```python
import jax
import jax.numpy as jnp
from jax import lax
from jax.sharding import PartitionSpec as P

BLK = 128


def expand(mask):
    return jnp.repeat(jnp.repeat(mask, BLK, axis=0), BLK, axis=1) > 0


def swiglu(sums):
    width = sums.shape[1] // 2
    gate = sums[:, :width]
    up = sums[:, width:]
    sig = jax.nn.sigmoid(gate)
    return (gate * sig * up).astype(jnp.bfloat16)


def swiglu_back(sums, grad_act):
    width = sums.shape[1] // 2
    gate = sums[:, :width]
    up = sums[:, width:]
    sig = jax.nn.sigmoid(gate)
    grad_gate = grad_act * up * sig * (1.0 + gate * (1.0 - sig))
    grad_up = grad_act * gate * sig
    return jnp.concatenate([grad_gate, grad_up], axis=1).astype(jnp.bfloat16)


def row_sums(term, rows):
    return lax.psum_scatter(
        term(jnp.int32(0), lax.axis_size("row") * rows), "row", scatter_dimension=0, tiled=True
    )


def row_gather(block):
    return lax.all_gather(block, "row", axis=0, tiled=True)


def row_sums_direct(full):
    parts = lax.axis_size("row")
    rows = full.shape[0] // parts
    pieces = lax.all_to_all(
        full.astype(jnp.bfloat16).reshape((parts, rows) + full.shape[1:]), "row", 0, 0
    )
    return jnp.sum(pieces.astype(jnp.float32), axis=0)


def row_sums_paired(full):
    parts = lax.axis_size("row")
    chips = parts // 2
    rows = full.shape[0] // parts
    member = lax.axis_index("row")
    core = member % 2
    chip = member // 2
    blocks = full.reshape((chips, 2, rows) + full.shape[1:])
    give = jnp.take(blocks, 1 - core, axis=1)
    keep = jnp.take(blocks, core, axis=1)
    moved_in = lax.ppermute(give.astype(jnp.bfloat16), "row", [(i, i ^ 1) for i in range(parts)])
    pair = keep + moved_in.astype(jnp.float32)
    sent = pair.astype(jnp.bfloat16)
    total = jnp.take(pair, chip, axis=0)
    for hop in range(1, chips):
        piece = jnp.take(sent, (chip + hop) % chips, axis=0)
        moved = lax.ppermute(piece, "row", [(i, (i + 2 * hop) % parts) for i in range(parts)])
        total = total + moved.astype(jnp.float32)
    return total


def row_gather_direct(block):
    parts = lax.axis_size("row")
    copies = jnp.broadcast_to(block[None], (parts,) + block.shape)
    pieces = lax.all_to_all(copies, "row", 0, 0)
    return pieces.reshape((parts * block.shape[0],) + block.shape[1:])


def group_sums(term, rows):
    parts = lax.axis_size(("col", "depth"))
    full = term(jnp.int32(0), rows * parts).astype(jnp.bfloat16)
    pieces = lax.all_to_all(full.reshape((parts, rows) + full.shape[1:]), ("col", "depth"), 0, 0)
    return jnp.sum(pieces.astype(jnp.float32), axis=0)


def group_gather(block):
    parts = lax.axis_size(("col", "depth"))
    copies = jnp.broadcast_to(block[None], (parts,) + block.shape)
    pieces = lax.all_to_all(copies, ("col", "depth"), 0, 0)
    return pieces.reshape((parts * block.shape[0],) + block.shape[1:])


def local(tokens, gate_weight, up_weight, down_weight, gate_mask, up_mask, down_mask, grad_out):
    zero_value = jnp.zeros((), jnp.bfloat16)
    keep_gate = expand(gate_mask)
    keep_up = expand(up_mask)
    keep_down = expand(down_mask)
    w_both = jnp.concatenate(
        [jnp.where(keep_gate, gate_weight, zero_value), jnp.where(keep_up, up_weight, zero_value)],
        axis=1,
    )
    w_down = jnp.where(keep_down, down_weight, zero_value)
    x_all = group_gather(tokens)
    split_rows = x_all.shape[0] // lax.axis_size("row")
    own_rows = tokens.shape[0]
    inner = (((0,), (0,)), ((), ()))
    outer = (((1,), (1,)), ((), ()))

    hidden = jnp.dot(x_all, w_both, preferred_element_type=jnp.float32)
    sums = row_sums(lambda start, count: hidden, split_rows)
    grad_out, _ = lax.optimization_barrier((grad_out, hidden))
    grad_all = group_gather(grad_out)
    act_partial = lax.dot_general(grad_all, w_down, outer, preferred_element_type=jnp.float32)
    act_sums, act_partial = lax.optimization_barrier((sums, act_partial))
    act_all = row_gather(swiglu(act_sums))

    def out_term(start, count):
        return jnp.dot(act_all, w_down, preferred_element_type=jnp.float32)

    mixed = group_sums(out_term, own_rows).astype(jnp.bfloat16)
    grad_down = lax.dot_general(act_all, grad_all, inner, preferred_element_type=jnp.float32)
    grad_down_weight = jnp.where(keep_down, grad_down, jnp.float32(0.0)).astype(jnp.bfloat16)

    grad_act = row_sums_paired(act_partial)
    held_sums, grad_act, _ = lax.optimization_barrier((sums, grad_act, act_all))
    grads_all = row_gather(swiglu_back(held_sums, grad_act))
    grad_both = lax.dot_general(x_all, grads_all, inner, preferred_element_type=jnp.float32)
    width = grad_both.shape[1] // 2
    grad_gate_weight = jnp.where(keep_gate, grad_both[:, :width], jnp.float32(0.0)).astype(
        jnp.bfloat16
    )
    grad_up_weight = jnp.where(keep_up, grad_both[:, width:], jnp.float32(0.0)).astype(jnp.bfloat16)

    def input_term(start, count):
        return lax.dot_general(grads_all, w_both, outer, preferred_element_type=jnp.float32)

    grad_tokens = group_sums(input_term, own_rows).astype(jnp.bfloat16)
    return (mixed, grad_tokens, grad_gate_weight, grad_up_weight, grad_down_weight)


def solution(mesh):
    return jax.shard_map(
        local,
        mesh=mesh,
        in_specs=(
            P(("col", "depth"), "row"),
            P("row", ("col", "depth")),
            P("row", ("col", "depth")),
            P(("col", "depth"), "row"),
            P("row", ("col", "depth")),
            P("row", ("col", "depth")),
            P(("col", "depth"), "row"),
            P(("col", "depth"), "row"),
        ),
        out_specs=(
            P(("col", "depth"), "row"),
            P(("col", "depth"), "row"),
            P("row", ("col", "depth")),
            P("row", ("col", "depth")),
            P(("col", "depth"), "row"),
        ),
        check_vma=False,
    )
```
